32 devices in a mesh: groups: 2 (over y), row: 8 (over z, x), col: 2 (over core).
Axes of the slice: x: 2, y: 2, z: 4, core: 2. Of those that a mesh axis runs over, the one named last changes fastest.
Arguments:
- feature_map: bfloat16 [256, 64, 256], P(('groups', 'row'), 'col'), parts along dimension 0, may hold values from -6 to 6
- cotangent: bfloat16 [256, 64, 256], P(('groups', 'row'), 'col'), parts along dimension 0, may hold values from -6 to 6
- kernel: float32 [49, 256], replicated, may hold values from -0.875 to 0.875
- kernel_bias: float32 [256], replicated, may hold values from -3 to 3
- norm_gain: float32 [256], replicated, may hold values from 0.25 to 1.75
- norm_bias: float32 [256], replicated, may hold values from -3 to 3
- weight_in: bfloat16 [256, 1024], replicated, may hold values from -0.375 to 0.375
- bias_in: float32 [1024], replicated, may hold values from -3 to 3
- weight_out: bfloat16 [1024, 256], replicated, may hold values from -0.1875 to 0.1875
- bias_out: float32 [256], replicated, may hold values from -3 to 3
- layer_scale: float32 [256], replicated, may hold values from 0.3 to 3
Outputs:
- grad_input: bfloat16 [256, 64, 256], P(('groups', 'row'), 'col'), parts along dimension 0
- grad_kernel: float32 [98, 256], P('groups'), parts along dimension 0
- grad_kernel_bias: float32 [512], P('groups'), parts along dimension 0
- grad_norm_gain: float32 [512], P('groups'), parts along dimension 0
- grad_norm_bias: float32 [512], P('groups'), parts along dimension 0
- grad_weight_in: float32 [512, 1024], P('groups'), parts along dimension 0
- grad_bias_in: float32 [2048], P('groups'), parts along dimension 0
- grad_weight_out: float32 [2048, 256], P('groups'), parts along dimension 0
- grad_bias_out: float32 [512], P('groups'), parts along dimension 0
- grad_layer_scale: float32 [512], P('groups'), parts along dimension 0
The draws below stay inside these ranges and needn't reach their ends.
There are 2 independent parts, one for each index of `groups`. The reference program is written for one: setup_inputs(seed, part) draws one part's arguments, and reference() takes and returns one part's arrays. A program takes and returns all parts, laid end to end along the dimension named above; an argument that names none is the same for every part. Nothing has to cross between parts.
All inputs are finite; a program needn't handle non-finite values.
Results may differ from the reference program's by a relative error of at most 0.0065.
Values may be sent and summed in bfloat16 or wider, within the bound.
No kernel may reach another device: no remote copies, remote signals or barrier semaphores. Data moves between devices by JAX's collectives and lax.ppermute only.
A program may use at most 64 MiB of HBM per device.

```python
import math
import jax
import jax.numpy as jnp
from jax import lax

C = 256
FF = 1024
KS = 7
HT = 16
WT = 32
H = 128
W = 64
N_ROW = 8


def steps_of(own_key, shape, pieces, low, top_value):
    factor_of = 1.0
    for axis_at, blocks in pieces:
        steps = jax.random.uniform(jax.random.fold_in(jax.random.fold_in(own_key, 6), axis_at), (blocks,), jnp.float32, low / len(pieces), top_value / len(pieces))
        factor_of = factor_of * jnp.repeat(jnp.exp(steps), shape[axis_at] // blocks).reshape((-1,) + (1,) * (len(shape) - 1 - axis_at))
    return factor_of


def gaussian(rng, extent, scale, limit, split=(), dtype=jnp.bfloat16):
    values = jax.random.normal(rng, extent, jnp.float32) * scale
    if len(split) > 0:
        values = steps_of(rng, extent, split, -0.22, 0.18) * values
    return jnp.clip(values, min=-limit, max=limit).astype(dtype)


def setup_inputs(seed: int = 0, part: int = 0) -> dict:
    keys = jax.random.split(jax.random.key(seed), 12)
    part_keys = jax.random.split(jax.random.fold_in(keys[11], part), 12)
    feature_map = gaussian(part_keys[0], (H, W, C), 1.0, 6.0, ((0, 8), (1, 2)))
    cotangent = gaussian(part_keys[1], (H, W, C), 1.0, 6.0, ((0, 8), (1, 2)))
    kernel = gaussian(keys[2], (KS * KS, C), (KS * KS) ** -0.5, 0.875, (), jnp.float32)
    kernel_bias = gaussian(keys[3], (C,), 0.5, 3.0, (), jnp.float32)
    norm_gain = jnp.clip(1.0 + 0.15 * jax.random.normal(keys[4], (C,), jnp.float32), 0.25, 1.75)
    norm_bias = gaussian(keys[5], (C,), 0.5, 3.0, (), jnp.float32)
    weight_in = gaussian(keys[6], (C, FF), C ** -0.5, 0.375)
    bias_in = gaussian(keys[7], (FF,), 0.5, 3.0, (), jnp.float32)
    weight_out = gaussian(keys[8], (FF, C), FF ** -0.5, 0.1875)
    bias_out = gaussian(keys[9], (C,), 0.5, 3.0, (), jnp.float32)
    layer_scale = jnp.clip(jnp.exp(jax.random.uniform(keys[10], (C,), jnp.float32, math.log(0.3), math.log(3.0))), 0.3, 3.0)
    return {"feature_map": feature_map, "cotangent": cotangent, "kernel": kernel, "kernel_bias": kernel_bias, "norm_gain": norm_gain, "norm_bias": norm_bias, "weight_in": weight_in, "bias_in": bias_in, "weight_out": weight_out, "bias_out": bias_out, "layer_scale": layer_scale}


def gelu_pair(pre_act):
    normal_cdf = 0.5 * (1.0 + lax.erf(pre_act * 0.7071067811865476))
    normal_pdf = jnp.exp(-0.5 * pre_act * pre_act) * 0.3989422804014327
    return (pre_act * normal_cdf, normal_cdf + pre_act * normal_pdf)

def depthwise(padded, kernel, row_count, col_count):
    running = jnp.zeros((row_count, col_count, kernel.shape[1]), jnp.float32)
    for tap_index in range(KS * KS):
        row_off, col_off = divmod(tap_index, KS)
        running = running + padded[row_off:row_off + row_count, col_off:col_off + col_count] * kernel[tap_index]
    return running

def reference(feature_map, cotangent, kernel, kernel_bias, norm_gain, norm_bias, weight_in, bias_in, weight_out, bias_out, layer_scale):
    height, breadth, channels = feature_map.shape
    hidden_units = weight_in.shape[1]
    padded = jnp.pad(feature_map, ((3, 3), (3, 3), (0, 0)))
    conv_out = depthwise(padded, kernel, height, breadth) + kernel_bias
    centred = conv_out - lax.optimization_barrier(jnp.mean(conv_out, axis=2, keepdims=True))
    inv_std = lax.rsqrt(lax.optimization_barrier(jnp.mean(centred * centred, axis=2, keepdims=True)) + 1e-06)
    normed = centred * inv_std
    scaled = (normed * norm_gain + norm_bias).astype(jnp.bfloat16)
    block_rows = HT * WT
    count_blocks = height * breadth // block_rows
    stacked_in = scaled.reshape(count_blocks, block_rows, channels)
    stacked_grad = cotangent.reshape(count_blocks, block_rows, channels)
    contract_last = (((1,), (1,)), ((), ()))
    contract_first = (((0,), (0,)), ((), ()))

    def block_step(running, block_items):
        flat_in, grad_block = block_items
        pre_act = jnp.dot(flat_in, weight_in, preferred_element_type=jnp.float32) + bias_in
        act_val, act_slope = gelu_pair(pre_act)
        hidden = act_val.astype(jnp.bfloat16)
        branch = jnp.dot(hidden, weight_out, preferred_element_type=jnp.float32) + bias_out
        upstream = grad_block.astype(jnp.float32)
        grad_branch = upstream * layer_scale
        grad_branch_b = grad_branch.astype(jnp.bfloat16)
        grad_hidden = lax.dot_general(grad_branch_b, weight_out, contract_last, preferred_element_type=jnp.float32)
        grad_pre = (grad_hidden * act_slope).astype(jnp.bfloat16)
        grad_scaled = lax.dot_general(grad_pre, weight_in, contract_last, preferred_element_type=jnp.float32)
        updated = (running[0] + lax.dot_general(flat_in, grad_pre, contract_first, preferred_element_type=jnp.float32), running[1] + lax.optimization_barrier(jnp.sum(grad_pre.astype(jnp.float32), axis=0)), running[2] + lax.dot_general(hidden, grad_branch_b, contract_first, preferred_element_type=jnp.float32), running[3] + lax.optimization_barrier(jnp.sum(grad_branch, axis=0)), running[4] + lax.optimization_barrier(jnp.sum(upstream * branch, axis=0)))
        return (updated, grad_scaled)
    start = (jnp.zeros((channels, hidden_units), jnp.float32), jnp.zeros((hidden_units,), jnp.float32), jnp.zeros((hidden_units, channels), jnp.float32), jnp.zeros((channels,), jnp.float32), jnp.zeros((channels,), jnp.float32))
    sums, grad_scaled = lax.scan(block_step, start, (stacked_in, stacked_grad))
    grad_scaled = grad_scaled.reshape(height, breadth, channels)
    grad_normed = grad_scaled * norm_gain
    grad_conv = (grad_normed - lax.optimization_barrier(jnp.mean(grad_normed, axis=2, keepdims=True)) - normed * lax.optimization_barrier(jnp.mean(grad_normed * normed, axis=2, keepdims=True))) * inv_std
    grad_gain = lax.optimization_barrier(jnp.sum(grad_scaled * normed, axis=(0, 1)))
    grad_shift = lax.optimization_barrier(jnp.sum(grad_scaled, axis=(0, 1)))
    tap_sums = []
    for tap_index in range(KS * KS):
        row_off, col_off = divmod(tap_index, KS)
        tap_sums.append(lax.optimization_barrier(jnp.sum(padded[row_off:row_off + height, col_off:col_off + breadth] * grad_conv, axis=(0, 1))))
    grad_kernel = jnp.stack(tap_sums)
    grad_kbias = lax.optimization_barrier(jnp.sum(grad_conv, axis=(0, 1)))
    grad_pad = jnp.pad(grad_conv, ((3, 3), (3, 3), (0, 0)))
    running_input = cotangent.astype(jnp.float32)
    for tap_index in range(KS * KS):
        row_off, col_off = divmod(tap_index, KS)
        running_input = running_input + grad_pad[6 - row_off:6 - row_off + height, 6 - col_off:6 - col_off + breadth] * kernel[tap_index]
    divisor = 4.0 * N_ROW
    return (running_input.astype(jnp.bfloat16), grad_kernel / divisor, grad_kbias / divisor, grad_gain / divisor, grad_shift / divisor, sums[0] / divisor, sums[1] / divisor, sums[2] / divisor, sums[3] / divisor, sums[4] / divisor)
```

```python
import functools

import jax
import jax.numpy as jnp
from jax import lax
import numpy as np
from jax.sharding import PartitionSpec as P

KS = 7


def with_halo(block, sides, width):
    for axis, dim in sides:
        count = lax.axis_size(axis)
        forward = [(i, i + 1) for i in range(count - 1)]
        backward = [(target, source) for source, target in forward]
        low = lax.ppermute(
            lax.slice_in_dim(block, block.shape[dim] - width, None, axis=dim), axis, forward
        )
        high = lax.ppermute(lax.slice_in_dim(block, 0, width, axis=dim), axis, backward)
        block = jnp.concatenate([low, block, high], axis=dim)
    return block


def gelu_pair(pre_act):
    normal_cdf = 0.5 * (1.0 + lax.erf(pre_act * 0.7071067811865476))
    normal_pdf = jnp.exp(-0.5 * pre_act * pre_act) * 0.3989422804014327
    return (pre_act * normal_cdf, normal_cdf + pre_act * normal_pdf)


def depthwise(padded, kernel, row_count, col_count):
    running = jnp.zeros((row_count, col_count, kernel.shape[1]), jnp.float32)
    for tap_index in range(KS * KS):
        row_off, col_off = divmod(tap_index, KS)
        running = (
            running
            + padded[row_off : row_off + row_count, col_off : col_off + col_count]
            * kernel[tap_index]
        )
    return running


def forward_back(
    padded,
    grad_view,
    kernel,
    kernel_bias,
    norm_gain,
    norm_bias,
    weight_in,
    bias_in,
    weight_out,
    bias_out,
    layer_scale,
):
    row_count, col_count, channels = grad_view.shape
    contract_last = (((1,), (1,)), ((), ()))
    conv_out = depthwise(padded, kernel, row_count, col_count) + kernel_bias
    centred = conv_out - jnp.mean(conv_out, axis=2, keepdims=True)
    inv_std = lax.rsqrt(jnp.mean(centred * centred, axis=2, keepdims=True) + 1e-06)
    normed = centred * inv_std
    flat_in = (normed * norm_gain + norm_bias).astype(jnp.bfloat16).reshape(-1, channels)
    pre_act = jnp.dot(flat_in, weight_in, preferred_element_type=jnp.float32) + bias_in
    act_val, act_slope = gelu_pair(pre_act)
    hidden = act_val.astype(jnp.bfloat16)
    branch = jnp.dot(hidden, weight_out, preferred_element_type=jnp.float32) + bias_out
    upstream = grad_view.reshape(-1, channels).astype(jnp.float32)
    grad_branch = upstream * layer_scale
    grad_branch_b = grad_branch.astype(jnp.bfloat16)
    grad_hidden = lax.dot_general(
        grad_branch_b, weight_out, contract_last, preferred_element_type=jnp.float32
    )
    grad_pre = (grad_hidden * act_slope).astype(jnp.bfloat16)
    grad_scaled = lax.dot_general(
        grad_pre, weight_in, contract_last, preferred_element_type=jnp.float32
    )
    grad_normed = grad_scaled.reshape(row_count, col_count, channels) * norm_gain
    grad_conv = (
        grad_normed
        - jnp.mean(grad_normed, axis=2, keepdims=True)
        - normed * jnp.mean(grad_normed * normed, axis=2, keepdims=True)
    ) * inv_std
    flat_parts = [
        flat_in,
        hidden,
        branch,
        upstream,
        grad_branch,
        grad_branch_b,
        grad_pre,
        grad_scaled,
    ]
    return (flat_parts, normed, grad_conv)


def ring_order(coords):
    count = len(coords)
    varying = [k for k in range(len(coords[0])) if len({c[k] for c in coords}) > 1]
    if len(varying) != 2:
        return sorted(range(count), key=lambda r: coords[r])
    ranks = []
    for k in varying:
        values = sorted({c[k] for c in coords})
        ranks.append({v: i for i, v in enumerate(values)})
    grid = {(ranks[0][c[varying[0]]], ranks[1][c[varying[1]]]): r for r, c in enumerate(coords)}
    size_a, size_b = len(ranks[0]), len(ranks[1])
    swap = size_a % 2 == 1
    if swap:
        size_a, size_b = size_b, size_a
    if size_a % 2 == 1 or size_a * size_b != count:
        return list(range(count))
    cycle = []
    for i in range(size_a):
        cols = range(1, size_b) if i % 2 == 0 else range(size_b - 1, 0, -1)
        cycle += [(i, j) for j in cols]
    cycle += [(i, 0) for i in range(size_a - 1, -1, -1)]
    if swap:
        cycle = [(j, i) for i, j in cycle]
    return [grid[cell] for cell in cycle]


def ring_position(axis, order):
    position_of = [0] * len(order)
    for position, member in enumerate(order):
        position_of[member] = position
    return jnp.asarray(position_of, jnp.int32)[lax.axis_index(axis)]


def ring_pairs(order, step):
    count = len(order)
    return [(order[i], order[(i + step) % count]) for i in range(count)]


def ring_reduce_scatter(block, axis, order, ways):
    count = len(order)
    if count == 1:
        return [block]
    here = ring_position(axis, order)
    part = block.shape[0] // (ways * count)
    chunks = block.reshape(ways, count, part, block.shape[1])
    signs = (1, -1)[:ways]

    def take(way, index):
        return lax.dynamic_index_in_dim(chunks[way], index % count, axis=0, keepdims=False)

    held = [take(way, here) for way in range(ways)]
    for step in range(count - 1):
        held = [
            lax.ppermute(held[way], axis, ring_pairs(order, signs[way]))
            + take(way, here - signs[way] * (1 + step))
            for way in range(ways)
        ]
    return held


def ring_all_gather(held, axis, order):
    count = len(order)
    if count == 1:
        return held[0]
    here = ring_position(axis, order)
    signs = (1, -1)[: len(held)]
    gathered = []
    for way, piece in enumerate(held):
        sign = signs[way]
        full = jnp.zeros((count,) + piece.shape, piece.dtype)
        full = lax.dynamic_update_index_in_dim(full, piece, (here + sign) % count, axis=0)
        for step in range(count - 1):
            piece = lax.ppermute(piece, axis, ring_pairs(order, sign))
            full = lax.dynamic_update_index_in_dim(full, piece, (here - sign * step) % count, axis=0)
        gathered.append(full)
    stacked = jnp.stack(gathered)
    return stacked.reshape(-1, stacked.shape[-1])


def ring_all_reduce(block, row_order, col_order):
    block = ring_reduce_scatter(block, "col", col_order, 1)[0]
    held = ring_reduce_scatter(block, "row", row_order, 2)
    block = ring_all_gather(held, "row", row_order)
    return ring_all_gather([block], "col", col_order)


def per_device(
    row_order,
    col_order,
    feature_map,
    cotangent,
    kernel,
    kernel_bias,
    norm_gain,
    norm_bias,
    weight_in,
    bias_in,
    weight_out,
    bias_out,
    layer_scale,
):
    tile_rows, tile_cols, channels = feature_map.shape
    contract_first = (((0,), (0,)), ((), ()))
    padded = with_halo(feature_map, (("row", 0), ("col", 1)), 3)
    flat_parts, normed_full, grad_conv_full = forward_back(
        padded,
        cotangent,
        kernel,
        kernel_bias,
        norm_gain,
        norm_bias,
        weight_in,
        bias_in,
        weight_out,
        bias_out,
        layer_scale,
    )
    trimmed = [element for element in flat_parts]
    flat_in, hidden, branch, upstream, grad_branch, grad_branch_b, grad_pre, grad_scaled = trimmed
    grad_w_in = lax.dot_general(
        grad_pre, flat_in, contract_first, preferred_element_type=jnp.float32
    )
    grad_b_in = jnp.sum(grad_pre.astype(jnp.float32), axis=0)
    grad_w_out = lax.dot_general(
        hidden, grad_branch_b, contract_first, preferred_element_type=jnp.float32
    )
    grad_b_out = jnp.sum(grad_branch, axis=0)
    grad_scale = jnp.sum(upstream * branch, axis=0)
    grad_pad = with_halo(grad_conv_full, (("row", 0), ("col", 1)), 3)
    grad_gain = jnp.sum(grad_scaled * normed_full.reshape(-1, channels), axis=0)
    grad_shift = jnp.sum(grad_scaled, axis=0)
    tap_sums = []
    for tap_index in range(KS * KS):
        row_off, col_off = divmod(tap_index, KS)
        tap_sums.append(
            jnp.sum(
                padded[row_off : row_off + tile_rows, col_off : col_off + tile_cols]
                * grad_conv_full,
                axis=(0, 1),
            )
        )
    grad_kernel = lax.optimization_barrier(jnp.stack(tap_sums))
    grad_kbias = jnp.sum(grad_conv_full, axis=(0, 1))
    running_input = cotangent.astype(jnp.float32)
    for tap_index in range(KS * KS):
        row_off, col_off = divmod(tap_index, KS)
        running_input = (
            running_input
            + grad_pad[6 - row_off : 6 - row_off + tile_rows, 6 - col_off : 6 - col_off + tile_cols]
            * kernel[tap_index]
        )
    divisor = 4.0 * lax.axis_size("row")
    pieces = [
        grad_w_in,
        grad_w_out,
        grad_kernel,
        grad_kbias,
        grad_gain,
        grad_shift,
        grad_b_in,
        grad_b_out,
        grad_scale,
    ]
    flat = [piece.reshape(-1, channels) for piece in pieces]
    rows = sum(piece.shape[0] for piece in flat)
    unit = 2 * 8 * len(row_order) * len(col_order)
    flat.append(jnp.zeros(((-rows) % unit, channels), jnp.float32))
    packed = ring_all_reduce(jnp.concatenate(flat, axis=0), row_order, col_order)
    totals = []
    at = 0
    for piece in pieces:
        count = piece.size // channels
        part = packed[at : at + count]
        if piece is grad_w_in:
            part = part.T
        totals.append(part.reshape(piece.shape if piece is not grad_w_in else (channels, -1)) / divisor)
        at += count
    (w_in, w_out, g_kernel, g_kbias, g_gain, g_shift, g_b_in, g_b_out, g_scale) = totals
    return (
        running_input.astype(jnp.bfloat16),
        g_kernel,
        g_kbias,
        g_gain,
        g_shift,
        w_in,
        g_b_in,
        w_out,
        g_b_out,
        g_scale,
    )


def solution(mesh):
    in_specs = (
        P(("groups", "row"), "col", None),
        P(("groups", "row"), "col", None),
        P(),
        P(),
        P(),
        P(),
        P(),
        P(),
        P(),
        P(),
        P(),
    )
    out_specs = (
        P(("groups", "row"), "col", None),
        P("groups", None),
        P("groups"),
        P("groups"),
        P("groups"),
        P("groups", None),
        P("groups"),
        P("groups", None),
        P("groups"),
        P("groups"),
    )
    devices = mesh.devices
    row_at = mesh.axis_names.index("row")
    col_at = mesh.axis_names.index("col")
    row_members = np.moveaxis(devices, row_at, 0).reshape(devices.shape[row_at], -1)[:, 0]
    row_order = ring_order([tuple(device.coords) for device in row_members])
    col_order = list(range(devices.shape[col_at]))
    return jax.shard_map(
        functools.partial(per_device, row_order, col_order), mesh=mesh, in_specs=in_specs, out_specs=out_specs, check_vma=False
    )
```

```python
import functools

import jax
import jax.numpy as jnp
from jax import lax
import numpy as np
from jax.sharding import PartitionSpec as P

KS = 7


def with_halo(block, sides, width):
    for axis, dim in sides:
        count = lax.axis_size(axis)
        forward = [(i, i + 1) for i in range(count - 1)]
        backward = [(target, source) for source, target in forward]
        low = lax.ppermute(
            lax.slice_in_dim(block, block.shape[dim] - width, None, axis=dim), axis, forward
        )
        high = lax.ppermute(lax.slice_in_dim(block, 0, width, axis=dim), axis, backward)
        block = jnp.concatenate([low, block, high], axis=dim)
    return block


def gelu_pair(pre_act):
    normal_cdf = 0.5 * (1.0 + lax.erf(pre_act * 0.7071067811865476))
    normal_pdf = jnp.exp(-0.5 * pre_act * pre_act) * 0.3989422804014327
    return (pre_act * normal_cdf, normal_cdf + pre_act * normal_pdf)


def depthwise(padded, kernel, row_count, col_count):
    running = jnp.zeros((row_count, col_count, kernel.shape[1]), jnp.float32)
    for tap_index in range(KS * KS):
        row_off, col_off = divmod(tap_index, KS)
        running = (
            running
            + padded[row_off : row_off + row_count, col_off : col_off + col_count]
            * kernel[tap_index]
        )
    return running


def forward_back(
    padded,
    grad_view,
    kernel,
    kernel_bias,
    norm_gain,
    norm_bias,
    weight_in,
    bias_in,
    weight_out,
    bias_out,
    layer_scale,
):
    row_count, col_count, channels = grad_view.shape
    contract_last = (((1,), (1,)), ((), ()))
    conv_out = depthwise(padded, kernel, row_count, col_count) + kernel_bias
    centred = conv_out - jnp.mean(conv_out, axis=2, keepdims=True)
    inv_std = lax.rsqrt(jnp.mean(centred * centred, axis=2, keepdims=True) + 1e-06)
    normed = centred * inv_std
    flat_in = (normed * norm_gain + norm_bias).astype(jnp.bfloat16).reshape(-1, channels)
    pre_act = jnp.dot(flat_in, weight_in, preferred_element_type=jnp.float32) + bias_in
    act_val, act_slope = gelu_pair(pre_act)
    hidden = act_val.astype(jnp.bfloat16)
    branch = jnp.dot(hidden, weight_out, preferred_element_type=jnp.float32) + bias_out
    upstream = grad_view.reshape(-1, channels).astype(jnp.float32)
    grad_branch = upstream * layer_scale
    grad_branch_b = grad_branch.astype(jnp.bfloat16)
    grad_hidden = lax.dot_general(
        grad_branch_b, weight_out, contract_last, preferred_element_type=jnp.float32
    )
    grad_pre = (grad_hidden * act_slope).astype(jnp.bfloat16)
    grad_scaled = lax.dot_general(
        grad_pre, weight_in, contract_last, preferred_element_type=jnp.float32
    )
    grad_normed = grad_scaled.reshape(row_count, col_count, channels) * norm_gain
    grad_conv = (
        grad_normed
        - jnp.mean(grad_normed, axis=2, keepdims=True)
        - normed * jnp.mean(grad_normed * normed, axis=2, keepdims=True)
    ) * inv_std
    flat_parts = [
        flat_in,
        hidden,
        branch,
        upstream,
        grad_branch,
        grad_branch_b,
        grad_pre,
        grad_scaled,
    ]
    return (flat_parts, normed, grad_conv)


def ring_order(coords):
    count = len(coords)
    varying = [k for k in range(len(coords[0])) if len({c[k] for c in coords}) > 1]
    if len(varying) != 2:
        return sorted(range(count), key=lambda r: coords[r])
    ranks = []
    for k in varying:
        values = sorted({c[k] for c in coords})
        ranks.append({v: i for i, v in enumerate(values)})
    grid = {(ranks[0][c[varying[0]]], ranks[1][c[varying[1]]]): r for r, c in enumerate(coords)}
    size_a, size_b = len(ranks[0]), len(ranks[1])
    swap = size_a % 2 == 1
    if swap:
        size_a, size_b = size_b, size_a
    if size_a % 2 == 1 or size_a * size_b != count:
        return list(range(count))
    cycle = []
    for i in range(size_a):
        cols = range(1, size_b) if i % 2 == 0 else range(size_b - 1, 0, -1)
        cycle += [(i, j) for j in cols]
    cycle += [(i, 0) for i in range(size_a - 1, -1, -1)]
    if swap:
        cycle = [(j, i) for i, j in cycle]
    return [grid[cell] for cell in cycle]


def ring_position(axis, order):
    position_of = [0] * len(order)
    for position, member in enumerate(order):
        position_of[member] = position
    return jnp.asarray(position_of, jnp.int32)[lax.axis_index(axis)]


def ring_pairs(order, step):
    count = len(order)
    return [(order[i], order[(i + step) % count]) for i in range(count)]


def ring_reduce_scatter(block, axis, order, ways):
    count = len(order)
    if count == 1:
        return [block]
    here = ring_position(axis, order)
    part = block.shape[0] // (ways * count)
    chunks = block.reshape(ways, count, part, block.shape[1])
    signs = (1, -1)[:ways]

    def take(way, index):
        return lax.dynamic_index_in_dim(chunks[way], index % count, axis=0, keepdims=False)

    held = [take(way, here) for way in range(ways)]
    for step in range(count - 1):
        held = [
            lax.ppermute(held[way], axis, ring_pairs(order, signs[way]))
            + take(way, here - signs[way] * (1 + step))
            for way in range(ways)
        ]
    return held


def ring_all_gather(held, axis, order):
    count = len(order)
    if count == 1:
        return held[0]
    here = ring_position(axis, order)
    signs = (1, -1)[: len(held)]
    gathered = []
    for way, piece in enumerate(held):
        sign = signs[way]
        full = jnp.zeros((count,) + piece.shape, piece.dtype)
        full = lax.dynamic_update_index_in_dim(full, piece, (here + sign) % count, axis=0)
        for step in range(count - 1):
            piece = lax.ppermute(piece, axis, ring_pairs(order, sign))
            full = lax.dynamic_update_index_in_dim(full, piece, (here - sign * step) % count, axis=0)
        gathered.append(full)
    stacked = jnp.stack(gathered)
    return stacked.reshape(-1, stacked.shape[-1])


def halving_stages(sizes):
    stages = []
    for axis, count in sizes:
        bit = 1
        while bit < count:
            stages.append((axis, count, bit))
            bit *= 2
    return stages


def stage_side(axis, bit):
    return (lax.axis_index(axis) // bit) % 2


def stage_pairs(count, bit):
    return [(i, i ^ bit) for i in range(count)]


def halving_reduce_scatter(block, stages):
    for axis, count, bit in stages:
        half = block.shape[0] // 2
        side = stage_side(axis, bit)
        kept = lax.dynamic_slice_in_dim(block, side * half, half, axis=0)
        sent = lax.dynamic_slice_in_dim(block, (1 - side) * half, half, axis=0)
        block = kept + lax.ppermute(sent, axis, stage_pairs(count, bit))
    return block


def doubling_all_gather(block, stages):
    for axis, count, bit in reversed(stages):
        side = stage_side(axis, bit)
        other = lax.ppermute(block, axis, stage_pairs(count, bit))
        full = jnp.zeros((2 * block.shape[0],) + block.shape[1:], block.dtype)
        full = lax.dynamic_update_slice_in_dim(full, block, side * block.shape[0], axis=0)
        block = lax.dynamic_update_slice_in_dim(full, other, (1 - side) * block.shape[0], axis=0)
    return block


def ring_all_reduce(block, row_order, col_order):
    stages = halving_stages((("col", len(col_order)), ("row", len(row_order))))
    block = halving_reduce_scatter(block, stages)
    return doubling_all_gather(block.astype(jnp.bfloat16), stages).astype(jnp.float32)


def per_device(
    row_order,
    col_order,
    feature_map,
    cotangent,
    kernel,
    kernel_bias,
    norm_gain,
    norm_bias,
    weight_in,
    bias_in,
    weight_out,
    bias_out,
    layer_scale,
):
    tile_rows, tile_cols, channels = feature_map.shape
    contract_first = (((0,), (0,)), ((), ()))
    padded = with_halo(feature_map, (("row", 0), ("col", 1)), 3)
    flat_parts, normed_full, grad_conv_full = forward_back(
        padded,
        cotangent,
        kernel,
        kernel_bias,
        norm_gain,
        norm_bias,
        weight_in,
        bias_in,
        weight_out,
        bias_out,
        layer_scale,
    )
    trimmed = [element for element in flat_parts]
    flat_in, hidden, branch, upstream, grad_branch, grad_branch_b, grad_pre, grad_scaled = trimmed
    grad_w_in = lax.dot_general(
        grad_pre, flat_in, contract_first, preferred_element_type=jnp.float32
    )
    grad_b_in = jnp.sum(grad_pre.astype(jnp.float32), axis=0)
    grad_w_out = lax.dot_general(
        hidden, grad_branch_b, contract_first, preferred_element_type=jnp.float32
    )
    grad_b_out = jnp.sum(grad_branch, axis=0)
    grad_scale = jnp.sum(upstream * branch, axis=0)
    grad_pad = with_halo(grad_conv_full, (("row", 0), ("col", 1)), 3)
    grad_gain = jnp.sum(grad_scaled * normed_full.reshape(-1, channels), axis=0)
    grad_shift = jnp.sum(grad_scaled, axis=0)
    tap_sums = []
    for tap_index in range(KS * KS):
        row_off, col_off = divmod(tap_index, KS)
        tap_sums.append(
            jnp.sum(
                padded[row_off : row_off + tile_rows, col_off : col_off + tile_cols]
                * grad_conv_full,
                axis=(0, 1),
            )
        )
    grad_kernel = lax.optimization_barrier(jnp.stack(tap_sums))
    grad_kbias = jnp.sum(grad_conv_full, axis=(0, 1))
    running_input = cotangent.astype(jnp.float32)
    for tap_index in range(KS * KS):
        row_off, col_off = divmod(tap_index, KS)
        running_input = (
            running_input
            + grad_pad[6 - row_off : 6 - row_off + tile_rows, 6 - col_off : 6 - col_off + tile_cols]
            * kernel[tap_index]
        )
    divisor = 4.0 * lax.axis_size("row")
    pieces = [
        grad_w_in,
        grad_w_out,
        grad_kernel,
        grad_kbias,
        grad_gain,
        grad_shift,
        grad_b_in,
        grad_b_out,
        grad_scale,
    ]
    flat = [piece.reshape(-1, channels) for piece in pieces]
    rows = sum(piece.shape[0] for piece in flat)
    unit = 2 * 8 * len(row_order) * len(col_order)
    flat.append(jnp.zeros(((-rows) % unit, channels), jnp.float32))
    packed = ring_all_reduce(jnp.concatenate(flat, axis=0), row_order, col_order)
    totals = []
    at = 0
    for piece in pieces:
        count = piece.size // channels
        part = packed[at : at + count]
        if piece is grad_w_in:
            part = part.T
        totals.append(part.reshape(piece.shape if piece is not grad_w_in else (channels, -1)) / divisor)
        at += count
    (w_in, w_out, g_kernel, g_kbias, g_gain, g_shift, g_b_in, g_b_out, g_scale) = totals
    return (
        running_input.astype(jnp.bfloat16),
        g_kernel,
        g_kbias,
        g_gain,
        g_shift,
        w_in,
        g_b_in,
        w_out,
        g_b_out,
        g_scale,
    )


def solution(mesh):
    in_specs = (
        P(("groups", "row"), "col", None),
        P(("groups", "row"), "col", None),
        P(),
        P(),
        P(),
        P(),
        P(),
        P(),
        P(),
        P(),
        P(),
    )
    out_specs = (
        P(("groups", "row"), "col", None),
        P("groups", None),
        P("groups"),
        P("groups"),
        P("groups"),
        P("groups", None),
        P("groups"),
        P("groups", None),
        P("groups"),
        P("groups"),
    )
    devices = mesh.devices
    row_at = mesh.axis_names.index("row")
    col_at = mesh.axis_names.index("col")
    row_members = np.moveaxis(devices, row_at, 0).reshape(devices.shape[row_at], -1)[:, 0]
    row_order = ring_order([tuple(device.coords) for device in row_members])
    col_order = list(range(devices.shape[col_at]))
    return jax.shard_map(
        functools.partial(per_device, row_order, col_order), mesh=mesh, in_specs=in_specs, out_specs=out_specs, check_vma=False
    )
```

```python
import jax
import jax.numpy as jnp
from jax import lax
from jax.sharding import PartitionSpec as P

KS = 7


def with_halo(block, sides, width):
    for axis, dim in sides:
        count = lax.axis_size(axis)
        forward = [(i, i + 1) for i in range(count - 1)]
        backward = [(target, source) for source, target in forward]
        low = lax.ppermute(
            lax.slice_in_dim(block, block.shape[dim] - width, None, axis=dim), axis, forward
        )
        high = lax.ppermute(lax.slice_in_dim(block, 0, width, axis=dim), axis, backward)
        block = jnp.concatenate([low, block, high], axis=dim)
    return block


def gelu_pair(pre_act):
    normal_cdf = 0.5 * (1.0 + lax.erf(pre_act * 0.7071067811865476))
    normal_pdf = jnp.exp(-0.5 * pre_act * pre_act) * 0.3989422804014327
    return (pre_act * normal_cdf, normal_cdf + pre_act * normal_pdf)


def depthwise(padded, kernel, row_count, col_count):
    running = jnp.zeros((row_count, col_count, kernel.shape[1]), jnp.float32)
    for tap_index in range(KS * KS):
        row_off, col_off = divmod(tap_index, KS)
        running = (
            running
            + padded[row_off : row_off + row_count, col_off : col_off + col_count]
            * kernel[tap_index]
        )
    return running


def forward_back(
    padded,
    grad_view,
    kernel,
    kernel_bias,
    norm_gain,
    norm_bias,
    weight_in,
    bias_in,
    weight_out,
    bias_out,
    layer_scale,
):
    row_count, col_count, channels = grad_view.shape
    contract_last = (((1,), (1,)), ((), ()))
    conv_out = depthwise(padded, kernel, row_count, col_count) + kernel_bias
    centred = conv_out - jnp.mean(conv_out, axis=2, keepdims=True)
    inv_std = lax.rsqrt(jnp.mean(centred * centred, axis=2, keepdims=True) + 1e-06)
    normed = centred * inv_std
    flat_in = (normed * norm_gain + norm_bias).astype(jnp.bfloat16).reshape(-1, channels)
    pre_act = jnp.dot(flat_in, weight_in, preferred_element_type=jnp.float32) + bias_in
    act_val, act_slope = gelu_pair(pre_act)
    hidden = act_val.astype(jnp.bfloat16)
    branch = jnp.dot(hidden, weight_out, preferred_element_type=jnp.float32) + bias_out
    upstream = grad_view.reshape(-1, channels).astype(jnp.float32)
    grad_branch = upstream * layer_scale
    grad_branch_b = grad_branch.astype(jnp.bfloat16)
    grad_hidden = lax.dot_general(
        grad_branch_b, weight_out, contract_last, preferred_element_type=jnp.float32
    )
    grad_pre = (grad_hidden * act_slope).astype(jnp.bfloat16)
    grad_scaled = lax.dot_general(
        grad_pre, weight_in, contract_last, preferred_element_type=jnp.float32
    )
    grad_normed = grad_scaled.reshape(row_count, col_count, channels) * norm_gain
    grad_conv = (
        grad_normed
        - jnp.mean(grad_normed, axis=2, keepdims=True)
        - normed * jnp.mean(grad_normed * normed, axis=2, keepdims=True)
    ) * inv_std
    flat_parts = [
        flat_in,
        hidden,
        branch,
        upstream,
        grad_branch,
        grad_branch_b,
        grad_pre,
        grad_scaled,
    ]
    return (flat_parts, normed, grad_conv)


def halving_stages(sizes):
    stages = []
    for axis, count in sizes:
        bit = 1
        while bit < count:
            stages.append((axis, count, bit))
            bit *= 2
    return stages


def stage_side(axis, bit):
    return (lax.axis_index(axis) // bit) % 2


def stage_pairs(count, bit):
    return [(i, i ^ bit) for i in range(count)]


def halving_reduce_scatter(block, stages):
    for axis, count, bit in stages:
        half = block.shape[0] // 2
        side = stage_side(axis, bit)
        kept = lax.dynamic_slice_in_dim(block, side * half, half, axis=0)
        sent = lax.dynamic_slice_in_dim(block, (1 - side) * half, half, axis=0)
        block = kept + lax.ppermute(sent, axis, stage_pairs(count, bit))
    return block


def doubling_all_gather(block, stages):
    for axis, count, bit in reversed(stages):
        side = stage_side(axis, bit)
        other = lax.ppermute(block, axis, stage_pairs(count, bit))
        full = jnp.zeros((2 * block.shape[0],) + block.shape[1:], block.dtype)
        full = lax.dynamic_update_slice_in_dim(full, block, side * block.shape[0], axis=0)
        block = lax.dynamic_update_slice_in_dim(full, other, (1 - side) * block.shape[0], axis=0)
    return block


def group_all_reduce(block, sizes, scale):
    stages = halving_stages(sizes)
    block = halving_reduce_scatter(block, stages) * scale
    return doubling_all_gather(block.astype(jnp.bfloat16), stages).astype(jnp.float32)


def pack_rows(pieces, channels, unit):
    flat = [piece.reshape(-1, channels) for piece in pieces]
    rows = sum(piece.shape[0] for piece in flat)
    if rows % unit:
        flat.append(jnp.zeros(((-rows) % unit, channels), jnp.float32))
    return jnp.concatenate(flat, axis=0)


def unpack_rows(packed, pieces, channels):
    parts = []
    at = 0
    for piece in pieces:
        count = piece.size // channels
        parts.append(packed[at : at + count].reshape(piece.shape))
        at += count
    return parts


def per_device(
    feature_map,
    cotangent,
    kernel,
    kernel_bias,
    norm_gain,
    norm_bias,
    weight_in,
    bias_in,
    weight_out,
    bias_out,
    layer_scale,
):
    tile_rows, tile_cols, channels = feature_map.shape
    contract_first = (((0,), (0,)), ((), ()))
    padded = with_halo(feature_map, (("row", 0), ("col", 1)), 3)
    flat_parts, normed_full, grad_conv_full = forward_back(
        padded,
        cotangent,
        kernel,
        kernel_bias,
        norm_gain,
        norm_bias,
        weight_in,
        bias_in,
        weight_out,
        bias_out,
        layer_scale,
    )
    trimmed = [element for element in flat_parts]
    flat_in, hidden, branch, upstream, grad_branch, grad_branch_b, grad_pre, grad_scaled = trimmed
    grad_w_in = lax.dot_general(
        grad_pre, flat_in, contract_first, preferred_element_type=jnp.float32
    )
    grad_b_in = jnp.sum(grad_pre.astype(jnp.float32), axis=0)
    grad_w_out = lax.dot_general(
        hidden, grad_branch_b, contract_first, preferred_element_type=jnp.float32
    )
    grad_b_out = jnp.sum(grad_branch, axis=0)
    grad_scale = jnp.sum(upstream * branch, axis=0)
    grad_pad = with_halo(grad_conv_full, (("row", 0), ("col", 1)), 3)
    grad_gain = jnp.sum(grad_scaled * normed_full.reshape(-1, channels), axis=0)
    grad_shift = jnp.sum(grad_scaled, axis=0)
    tap_sums = []
    for tap_index in range(KS * KS):
        row_off, col_off = divmod(tap_index, KS)
        tap_sums.append(
            jnp.sum(
                padded[row_off : row_off + tile_rows, col_off : col_off + tile_cols]
                * grad_conv_full,
                axis=(0, 1),
            )
        )
    grad_kernel = lax.optimization_barrier(jnp.stack(tap_sums))
    grad_kbias = jnp.sum(grad_conv_full, axis=(0, 1))
    running_input = cotangent.astype(jnp.float32)
    for tap_index in range(KS * KS):
        row_off, col_off = divmod(tap_index, KS)
        running_input = (
            running_input
            + grad_pad[6 - row_off : 6 - row_off + tile_rows, 6 - col_off : 6 - col_off + tile_cols]
            * kernel[tap_index]
        )
    divisor = 4.0 * lax.axis_size("row")
    sizes = (("col", lax.axis_size("col")), ("row", lax.axis_size("row")))
    unit = 8 * lax.axis_size("col") * lax.axis_size("row")
    early = [grad_b_in, grad_b_out, grad_scale]
    early_block = pack_rows(early, channels, 8)
    packed = pack_rows([grad_w_out, early_block], channels, unit)
    packed = group_all_reduce(packed, sizes, 1.0 / divisor)
    w_out, early_block = unpack_rows(packed, [grad_w_out, early_block], channels)
    g_b_in, g_b_out, g_scale = unpack_rows(early_block, early, channels)
    late = [grad_kernel, grad_kbias, grad_gain, grad_shift]
    late_block = pack_rows(late, channels, 8)
    packed = pack_rows([grad_w_in, late_block], channels, unit)
    packed = group_all_reduce(packed, sizes, 1.0 / divisor)
    w_in, late_block = unpack_rows(packed, [grad_w_in, late_block], channels)
    w_in = w_in.T
    g_kernel, g_kbias, g_gain, g_shift = unpack_rows(late_block, late, channels)
    return (
        running_input.astype(jnp.bfloat16),
        g_kernel,
        g_kbias,
        g_gain,
        g_shift,
        w_in,
        g_b_in,
        w_out,
        g_b_out,
        g_scale,
    )


def solution(mesh):
    in_specs = (
        P(("groups", "row"), "col", None),
        P(("groups", "row"), "col", None),
        P(),
        P(),
        P(),
        P(),
        P(),
        P(),
        P(),
        P(),
        P(),
    )
    out_specs = (
        P(("groups", "row"), "col", None),
        P("groups", None),
        P("groups"),
        P("groups"),
        P("groups"),
        P("groups", None),
        P("groups"),
        P("groups", None),
        P("groups"),
        P("groups"),
    )
    return jax.shard_map(
        per_device, mesh=mesh, in_specs=in_specs, out_specs=out_specs, check_vma=False
    )
```

```python
import jax
import jax.numpy as jnp
from jax import lax
from jax.sharding import PartitionSpec as P

KS = 7


def with_halo(block, sides, width):
    for axis, dim in sides:
        count = lax.axis_size(axis)
        forward = [(i, i + 1) for i in range(count - 1)]
        backward = [(target, source) for source, target in forward]
        low = lax.ppermute(
            lax.slice_in_dim(block, block.shape[dim] - width, None, axis=dim), axis, forward
        )
        high = lax.ppermute(lax.slice_in_dim(block, 0, width, axis=dim), axis, backward)
        block = jnp.concatenate([low, block, high], axis=dim)
    return block


def gelu_pair(pre_act):
    normal_cdf = 0.5 * (1.0 + lax.erf(pre_act * 0.7071067811865476))
    normal_pdf = jnp.exp(-0.5 * pre_act * pre_act) * 0.3989422804014327
    return (pre_act * normal_cdf, normal_cdf + pre_act * normal_pdf)


def depthwise(padded, kernel, row_count, col_count):
    running = jnp.zeros((row_count, col_count, kernel.shape[1]), jnp.float32)
    for tap_index in range(KS * KS):
        row_off, col_off = divmod(tap_index, KS)
        running = (
            running
            + padded[row_off : row_off + row_count, col_off : col_off + col_count]
            * kernel[tap_index]
        )
    return running


def forward_back(
    padded,
    grad_view,
    kernel,
    kernel_bias,
    norm_gain,
    norm_bias,
    weight_in,
    bias_in,
    weight_out,
    bias_out,
    layer_scale,
):
    row_count, col_count, channels = grad_view.shape
    contract_last = (((1,), (1,)), ((), ()))
    conv_out = depthwise(padded, kernel, row_count, col_count) + kernel_bias
    centred = conv_out - jnp.mean(conv_out, axis=2, keepdims=True)
    inv_std = lax.rsqrt(jnp.mean(centred * centred, axis=2, keepdims=True) + 1e-06)
    normed = centred * inv_std
    flat_in = (normed * norm_gain + norm_bias).astype(jnp.bfloat16).reshape(-1, channels)
    pre_act = jnp.dot(flat_in, weight_in, preferred_element_type=jnp.float32) + bias_in
    act_val, act_slope = gelu_pair(pre_act)
    hidden = act_val.astype(jnp.bfloat16)
    branch = jnp.dot(hidden, weight_out, preferred_element_type=jnp.float32) + bias_out
    upstream = grad_view.reshape(-1, channels).astype(jnp.float32)
    grad_branch = upstream * layer_scale
    grad_branch_b = grad_branch.astype(jnp.bfloat16)
    grad_hidden = lax.dot_general(
        grad_branch_b, weight_out, contract_last, preferred_element_type=jnp.float32
    )
    grad_pre = (grad_hidden * act_slope).astype(jnp.bfloat16)
    grad_scaled = lax.dot_general(
        grad_pre, weight_in, contract_last, preferred_element_type=jnp.float32
    )
    grad_normed = grad_scaled.reshape(row_count, col_count, channels) * norm_gain
    grad_conv = (
        grad_normed
        - jnp.mean(grad_normed, axis=2, keepdims=True)
        - normed * jnp.mean(grad_normed * normed, axis=2, keepdims=True)
    ) * inv_std
    flat_parts = [
        flat_in,
        hidden,
        branch,
        upstream,
        grad_branch,
        grad_branch_b,
        grad_pre,
        grad_scaled,
    ]
    return (flat_parts, normed, grad_conv)


def halving_stages(sizes):
    stages = []
    for axis, count in sizes:
        bit = 1
        while bit < count:
            stages.append((axis, count, bit))
            bit *= 2
    return stages


def stage_side(axis, bit):
    return (lax.axis_index(axis) // bit) % 2


def stage_pairs(count, bit):
    return [(i, i ^ bit) for i in range(count)]


def halving_reduce_scatter(block, stages):
    for axis, count, bit in stages:
        half = block.shape[0] // 2
        side = stage_side(axis, bit)
        kept = lax.dynamic_slice_in_dim(block, side * half, half, axis=0)
        sent = lax.dynamic_slice_in_dim(block, (1 - side) * half, half, axis=0)
        block = kept + lax.ppermute(sent, axis, stage_pairs(count, bit))
    return block


def doubling_all_gather(block, stages):
    for axis, count, bit in reversed(stages):
        side = stage_side(axis, bit)
        other = lax.ppermute(block, axis, stage_pairs(count, bit))
        full = jnp.zeros((2 * block.shape[0],) + block.shape[1:], block.dtype)
        full = lax.dynamic_update_slice_in_dim(full, block, side * block.shape[0], axis=0)
        block = lax.dynamic_update_slice_in_dim(full, other, (1 - side) * block.shape[0], axis=0)
    return block


def group_all_reduce(block, sizes, scale, swap=False):
    stages = halving_stages(sizes)
    if swap and len(stages) > 2:
        stages[1], stages[2] = stages[2], stages[1]
    block = halving_reduce_scatter(block, stages) * scale
    return doubling_all_gather(block.astype(jnp.bfloat16), stages).astype(jnp.float32)


def pack_rows(pieces, channels, unit):
    flat = [piece.reshape(-1, channels) for piece in pieces]
    rows = sum(piece.shape[0] for piece in flat)
    if rows % unit:
        flat.append(jnp.zeros(((-rows) % unit, channels), jnp.float32))
    return jnp.concatenate(flat, axis=0)


def unpack_rows(packed, pieces, channels):
    parts = []
    at = 0
    for piece in pieces:
        count = piece.size // channels
        parts.append(packed[at : at + count].reshape(piece.shape))
        at += count
    return parts


def per_device(
    feature_map,
    cotangent,
    kernel,
    kernel_bias,
    norm_gain,
    norm_bias,
    weight_in,
    bias_in,
    weight_out,
    bias_out,
    layer_scale,
):
    tile_rows, tile_cols, channels = feature_map.shape
    contract_first = (((0,), (0,)), ((), ()))
    padded = with_halo(feature_map, (("row", 0), ("col", 1)), 3)
    flat_parts, normed_full, grad_conv_full = forward_back(
        padded,
        cotangent,
        kernel,
        kernel_bias,
        norm_gain,
        norm_bias,
        weight_in,
        bias_in,
        weight_out,
        bias_out,
        layer_scale,
    )
    trimmed = [element for element in flat_parts]
    flat_in, hidden, branch, upstream, grad_branch, grad_branch_b, grad_pre, grad_scaled = trimmed
    grad_w_in = lax.dot_general(
        grad_pre, flat_in, contract_first, preferred_element_type=jnp.float32
    )
    grad_b_in = jnp.sum(grad_pre.astype(jnp.float32), axis=0)
    grad_w_out = lax.dot_general(
        hidden, grad_branch_b, contract_first, preferred_element_type=jnp.float32
    )
    grad_b_out = jnp.sum(grad_branch, axis=0)
    grad_scale = jnp.sum(upstream * branch, axis=0)
    grad_pad = with_halo(grad_conv_full, (("row", 0), ("col", 1)), 3)
    grad_gain = jnp.sum(grad_scaled * normed_full.reshape(-1, channels), axis=0)
    grad_shift = jnp.sum(grad_scaled, axis=0)
    tap_sums = []
    for tap_index in range(KS * KS):
        row_off, col_off = divmod(tap_index, KS)
        tap_sums.append(
            jnp.sum(
                padded[row_off : row_off + tile_rows, col_off : col_off + tile_cols]
                * grad_conv_full,
                axis=(0, 1),
            )
        )
    grad_kernel = lax.optimization_barrier(jnp.stack(tap_sums))
    grad_kbias = jnp.sum(grad_conv_full, axis=(0, 1))
    running_input = cotangent.astype(jnp.float32)
    for tap_index in range(KS * KS):
        row_off, col_off = divmod(tap_index, KS)
        running_input = (
            running_input
            + grad_pad[6 - row_off : 6 - row_off + tile_rows, 6 - col_off : 6 - col_off + tile_cols]
            * kernel[tap_index]
        )
    divisor = 4.0 * lax.axis_size("row")
    sizes = (("col", lax.axis_size("col")), ("row", lax.axis_size("row")))
    unit = 8 * lax.axis_size("col") * lax.axis_size("row")
    early = [grad_b_in, grad_b_out, grad_scale]
    early_block = pack_rows(early, channels, 8)
    packed = pack_rows([grad_w_out, early_block], channels, unit)
    packed = group_all_reduce(packed, sizes, 1.0 / divisor)
    w_out, early_block = unpack_rows(packed, [grad_w_out, early_block], channels)
    g_b_in, g_b_out, g_scale = unpack_rows(early_block, early, channels)
    late = [grad_kernel, grad_kbias, grad_gain, grad_shift]
    late_block = pack_rows(late, channels, 8)
    packed = pack_rows([grad_w_in, late_block], channels, unit)
    packed = group_all_reduce(packed, sizes, 1.0 / divisor, swap=True)
    w_in, late_block = unpack_rows(packed, [grad_w_in, late_block], channels)
    w_in = w_in.T
    g_kernel, g_kbias, g_gain, g_shift = unpack_rows(late_block, late, channels)
    return (
        running_input.astype(jnp.bfloat16),
        g_kernel,
        g_kbias,
        g_gain,
        g_shift,
        w_in,
        g_b_in,
        w_out,
        g_b_out,
        g_scale,
    )


def solution(mesh):
    in_specs = (
        P(("groups", "row"), "col", None),
        P(("groups", "row"), "col", None),
        P(),
        P(),
        P(),
        P(),
        P(),
        P(),
        P(),
        P(),
        P(),
    )
    out_specs = (
        P(("groups", "row"), "col", None),
        P("groups", None),
        P("groups"),
        P("groups"),
        P("groups"),
        P("groups", None),
        P("groups"),
        P("groups", None),
        P("groups"),
        P("groups"),
    )
    return jax.shard_map(
        per_device, mesh=mesh, in_specs=in_specs, out_specs=out_specs, check_vma=False
    )
```
